512 devices in a mesh: row: 16 (over x, y), col: 32 (over z, core).
Axes of the slice: x: 4, y: 4, z: 16, core: 2. Of those that a mesh axis runs over, the one named last changes fastest.
Arguments:
- hidden: bfloat16 [2560, 7168], P('col', 'row'), may hold values from -6 to 6
- ln_gain: bfloat16 [7168], P('row'), may hold values from 0.099609375 to 1.8984375
- ln_shift: bfloat16 [7168], P('row'), may hold values from -3 to 3
- qkv_weight: bfloat16 [7168, 12288], P('row', 'col'), may hold values from -0.0625 to 0.0625
- qkv_bias: bfloat16 [12288], P('col'), may hold values from -5.351432 to 5.351432
- out_weight: bfloat16 [4096, 7168], P('row', 'col'), may hold values from -0.09375 to 0.09375
- out_bias: bfloat16 [7168], P('col'), may hold values from -3 to 3
- down_qkv: bfloat16 [64, 7168, 16], P(None, 'row'), may hold values from -0.0625 to 0.0625
- up_qkv: bfloat16 [64, 16, 12288], P(None, None, 'col'), may hold values from -1.5 to 1.5
- down_out: bfloat16 [64, 16, 4096], P(None, None, 'col'), may hold values from -0.09375 to 0.09375
- up_out: bfloat16 [64, 16, 7168], P(None, None, 'col'), may hold values from -1.5 to 1.5
- prompt_lens: int32 [16], replicated, may hold values from 1 to 80, as said below
- suffix_lens: int32 [16, 16], replicated, may hold values from 1 to 5, as said below
- group_sizes: int32 [16], replicated, may hold values from 8 to 16, as said below
- group_adapter_choice: int32 [16], replicated, may hold values from 0 to 15
- chosen: int32 [16], replicated, may hold values from 0 to 63, as said below
Outputs:
- attn_out: bfloat16 [2560, 7168], P('row', 'col')
The draws below stay inside these ranges and needn't reach their ends.
Inputs may be any that keep to these rules, and one draw needn't show every extreme that they name: `prompt_lens`: one group, drawn from the seed, has a prompt of exactly 80 tokens, 16 requests and every suffix 5 long, so it fills all 160 slots. `suffix_lens`: entries past a group's number of requests are not used. `group_sizes`: A group's prompt and its live suffixes take at most 160 slots. `chosen`: 16 different bank indices.
All inputs are finite; a program needn't handle non-finite values.
Results may differ from the reference program's by a relative error of at most 0.012.
The reference program's roundings to bfloat16 on the way count: a program that leaves them out, or rounds other values in their place, can miss the bound.
Values may be sent and summed in bfloat16 or wider, within the bound.
No kernel may reach another device: no remote copies, remote signals or barrier semaphores. Data moves between devices by JAX's collectives and lax.ppermute only.
A program may use at most 64 MiB of HBM per device.

```python
import jax
import jax.numpy as jnp
from jax import lax

D = 7168
HEADS = 32
HEAD_SIZE = 128
RANK = 16
ADAPTER_COUNT = 64
CHOSEN_ADAPTERS = 16
RMAX = 16
GCAP = 160
HD = 4096
REQUEST_GROUPS = 16
TOKENS = 2560
S_MAX = 5
P_MAX = 80
WIN = 53


def busiest_group(key):
    return jax.random.randint(jax.random.fold_in(key, 9001), (), 0, REQUEST_GROUPS)


def draw_prompt_lens(key, part):
    busiest = busiest_group(key)
    sampled = jax.random.randint(jax.random.fold_in(key, 11), (REQUEST_GROUPS,), 1, P_MAX + 1)
    return jnp.where(jnp.arange(REQUEST_GROUPS) == busiest, P_MAX, sampled).astype(jnp.int32)


def draw_suffix_lens(key, part):
    busiest = busiest_group(key)
    sampled = jax.random.randint(jax.random.fold_in(key, 12), (REQUEST_GROUPS, RMAX), 1, S_MAX + 1)
    return jnp.where((jnp.arange(REQUEST_GROUPS) == busiest)[:, None], S_MAX, sampled).astype(jnp.int32)


def draw_group_sizes(key, part):
    busiest = busiest_group(key)
    sampled = jax.random.randint(jax.random.fold_in(key, 13), (REQUEST_GROUPS,), RMAX // 2, RMAX + 1)
    return jnp.where(jnp.arange(REQUEST_GROUPS) == busiest, RMAX, sampled).astype(jnp.int32)


def draw_chosen(key, part):
    return jax.random.permutation(jax.random.fold_in(key, 14), ADAPTER_COUNT)[:CHOSEN_ADAPTERS].astype(jnp.int32)


def draw_qkv_bias(key, part):
    base_key = jax.random.fold_in(key, 21)
    sign_key = jax.random.fold_in(key, 22)
    level_key = jax.random.fold_in(key, 23)
    pick_key = jax.random.fold_in(key, 24)
    place_key = jax.random.fold_in(key, 25)
    base = jnp.clip(0.5 * jax.random.normal(base_key, (HEADS, 3, HEAD_SIZE), jnp.float32), -3.0, 3.0)
    top_level = 15.0
    signs = jax.random.rademacher(sign_key, (HEADS, HEAD_SIZE)).astype(jnp.float32)
    drawn_levels = 11.0 + (top_level - 11.0) * jax.random.uniform(level_key, (HEADS,), jnp.float32)
    aligned_flag = jax.random.bernoulli(pick_key, 0.5, (HEADS,))
    forced = jax.random.randint(place_key, (), 0, HEADS)
    head_ids = jnp.arange(HEADS)
    level = jnp.where(aligned_flag, drawn_levels, 0.0)
    level = jnp.where(head_ids == (forced + 1) % HEADS, top_level, level)
    level = jnp.where(head_ids == forced, 0.0, level)
    aligned = (level * HEAD_SIZE ** (-0.25))[:, None] * signs
    hot_head = (level > 0.0)[:, None]
    query_part = jnp.where(hot_head, aligned, base[:, 0])
    key_part = jnp.where(hot_head, aligned, base[:, 1])
    stacked = jnp.stack([query_part, key_part, base[:, 2]], axis=1)
    return stacked.reshape(3 * HEADS * HEAD_SIZE).astype(jnp.bfloat16)


def touch_ends(array, own_key, smallest, top_value):
    dims = array.shape
    index_at = [jax.random.randint(jax.random.fold_in(own_key, axis), (), 0, dims[axis]) for axis in range(len(dims))]
    array = array.at[tuple(index_at)].set(smallest)
    longest = dims.index(max(dims))
    index_at[longest] = (index_at[longest] + 1) % dims[longest]
    return array.at[tuple(index_at)].set(top_value)


def block_scale(key, dims, cuts, smallest, largest):
    def one(axis_at, shards_of):
        draws = jax.random.uniform(jax.random.fold_in(jax.random.fold_in(key, 6), axis_at), (shards_of,), jnp.float32, smallest / len(cuts), largest / len(cuts))
        return jnp.repeat(jnp.exp(draws), dims[axis_at] // shards_of).reshape((-1,) + (1,) * (len(dims) - axis_at - 1))

    level = one(*cuts[0])
    for cut in cuts[1:]:
        level = level * one(*cut)
    return level


def gaussian(rng, dims, deviation, limit, cuts=(), held_as=jnp.bfloat16):
    loudness = block_scale(rng, dims, cuts, -0.22, 0.18) if cuts else 1.0
    array = jax.random.normal(rng, dims, jnp.float32) * deviation * loudness
    return jnp.minimum(jnp.maximum(array, -limit), limit).astype(held_as)


def setup_inputs(seed: int = 0) -> dict:
    seeds = jax.random.split(jax.random.key(seed), 17)
    hidden = gaussian(seeds[0], (TOKENS, D), 1.0, 6.0, ((0, 32), (1, 16)))
    ln_gain = jnp.clip(1.0 + 0.18 * jax.random.normal(seeds[1], (D,), jnp.float32), 0.099609375, 1.8984375).astype(jnp.bfloat16)
    ln_shift = gaussian(seeds[2], (D,), 0.5, 3.0, ((0, 16),))
    qkv_weight = gaussian(seeds[3], (D, 3 * HD), D ** -0.5, 0.0625, ((0, 16), (1, 32)))
    qkv_bias = draw_qkv_bias(jax.random.fold_in(seeds[16], 71), 0)
    out_weight = gaussian(seeds[5], (HD, D), HD ** -0.5, 0.09375, ((0, 16), (1, 32)))
    out_bias = gaussian(seeds[6], (D,), 0.5, 3.0, ((0, 32),))
    down_qkv = gaussian(seeds[7], (ADAPTER_COUNT, D, RANK), D ** -0.5, 0.0625, ((1, 16),))
    up_qkv = gaussian(seeds[8], (ADAPTER_COUNT, RANK, 3 * HD), RANK ** -0.5, 1.5, ((2, 32),))
    down_out = gaussian(seeds[9], (ADAPTER_COUNT, RANK, HD), HD ** -0.5, 0.09375, ((2, 32),))
    up_out = gaussian(seeds[10], (ADAPTER_COUNT, RANK, D), RANK ** -0.5, 1.5, ((2, 32),))
    prompt_lens = draw_prompt_lens(jax.random.fold_in(seeds[16], 71), 0)
    suffix_lens = draw_suffix_lens(jax.random.fold_in(seeds[16], 71), 0)
    group_sizes = draw_group_sizes(jax.random.fold_in(seeds[16], 71), 0)
    group_adapter_choice = touch_ends(jax.random.randint(seeds[14], (REQUEST_GROUPS,), 0, CHOSEN_ADAPTERS), jax.random.fold_in(seeds[14], 1), 0, CHOSEN_ADAPTERS - 1).astype(jnp.int32)
    chosen = draw_chosen(jax.random.fold_in(seeds[16], 71), 0)
    return dict(hidden=hidden, ln_gain=ln_gain, ln_shift=ln_shift, qkv_weight=qkv_weight, qkv_bias=qkv_bias, out_weight=out_weight, out_bias=out_bias, down_qkv=down_qkv, up_qkv=up_qkv, down_out=down_out, up_out=up_out, prompt_lens=prompt_lens, suffix_lens=suffix_lens, group_sizes=group_sizes, group_adapter_choice=group_adapter_choice, chosen=chosen)


def group_layout(prompt, count, suffix):
    offsets = jnp.arange(GCAP, dtype=jnp.int32)
    chosen_adapter_index = jnp.arange(suffix.shape[0], dtype=jnp.int32)
    live_lens = jnp.where(chosen_adapter_index < count, suffix, 0).astype(jnp.int32)
    end_at = (prompt + jnp.cumsum(live_lens)).astype(jnp.int32)
    group_start_rows = end_at - live_lens
    request = lax.optimization_barrier(jnp.sum((offsets[:, None] >= end_at[None, :]).astype(jnp.int32), axis=1))
    in_prompt = offsets < prompt
    live_rows = in_prompt | (request < count)
    group_begin_row = lax.optimization_barrier(jnp.sum(jnp.where(chosen_adapter_index[None, :] == request[:, None], group_start_rows[None, :], 0), axis=1)).astype(jnp.int32)
    position = jnp.where(in_prompt, offsets, prompt + offsets - group_begin_row).astype(jnp.int32)
    request_of = jnp.where(in_prompt, -1, request).astype(jnp.int32)
    return (live_rows, request_of, position)

def key_mask(live_rows, request_of, position):
    shared = (request_of[None, :] == -1) | (request_of[None, :] == request_of[:, None])
    causal = position[None, :] <= position[:, None]
    within = (position[:, None] - position[None, :] < WIN) | (position[None, :] == 0)
    allowed = live_rows[:, None] & live_rows[None, :] & shared & causal & within
    first_key = jnp.arange(GCAP)[None, :] == 0
    return jnp.where(live_rows[:, None], allowed, first_key)

def attention(queries, key_rows, value_rows, allowed):
    scores = jnp.einsum('qhe,khe->hqk', queries.astype(jnp.float32), key_rows.astype(jnp.float32))
    scores = jnp.where(allowed[None], scores, -1e+30)
    highest = lax.optimization_barrier(jnp.max(scores, axis=2, keepdims=True))
    weights = jnp.where(allowed[None], jnp.exp(scores - highest), 0.0)
    probs = (weights / lax.optimization_barrier(jnp.sum(weights, axis=2, keepdims=True))).astype(jnp.bfloat16)
    mixed_rows = jnp.einsum('hqk,khe->qhe', probs.astype(jnp.float32), value_rows.astype(jnp.float32))
    return mixed_rows.astype(jnp.bfloat16).reshape(queries.shape[0], -1)

def reference(hidden, ln_gain, ln_shift, qkv_weight, qkv_bias, out_weight, out_bias, down_qkv, up_qkv, down_out, up_out, prompt_lens, suffix_lens, group_sizes, group_adapter_choice, chosen):
    widened = hidden.astype(jnp.float32)
    average = lax.optimization_barrier(jnp.mean(widened, axis=1, keepdims=True))
    centred = widened - average
    spread = lax.optimization_barrier(jnp.mean(centred * centred, axis=1, keepdims=True))
    normed = (centred * lax.rsqrt(spread + 1e-05) * ln_gain.astype(jnp.float32) + ln_shift.astype(jnp.float32)).astype(jnp.bfloat16)
    adapters = chosen[group_adapter_choice]
    blocks = []
    for group_number in range(REQUEST_GROUPS):
        group_rows = normed[group_number * GCAP:(group_number + 1) * GCAP]
        own_adapter = adapters[group_number]
        projected = jnp.dot(group_rows, qkv_weight, preferred_element_type=jnp.float32)
        reduced = jnp.dot(group_rows, down_qkv[own_adapter], preferred_element_type=jnp.float32).astype(jnp.bfloat16)
        projected = projected + qkv_bias.astype(jnp.float32) + jnp.dot(reduced, up_qkv[own_adapter], preferred_element_type=jnp.float32)
        shaped = projected.reshape(GCAP, HEADS, 3, HEAD_SIZE)
        queries = (shaped[:, :, 0] * HEAD_SIZE ** (-0.5)).astype(jnp.bfloat16)
        key_rows = shaped[:, :, 1].astype(jnp.bfloat16)
        value_rows = shaped[:, :, 2].astype(jnp.bfloat16)
        live_rows, request_of, position = group_layout(prompt_lens[group_number], group_sizes[group_number], suffix_lens[group_number])
        mixed_rows = attention(queries, key_rows, value_rows, key_mask(live_rows, request_of, position))
        reduced_out = jnp.dot(mixed_rows, down_out[own_adapter].T, preferred_element_type=jnp.float32).astype(jnp.bfloat16)
        result = jnp.dot(mixed_rows, out_weight, preferred_element_type=jnp.float32) + out_bias.astype(jnp.float32)
        result = result + jnp.dot(reduced_out, up_out[own_adapter], preferred_element_type=jnp.float32)
        blocks.append((result * live_rows[:, None].astype(jnp.float32)).astype(jnp.bfloat16))
    return jnp.concatenate(blocks, axis=0)
```

```python
import jax
import jax.numpy as jnp
from jax import lax
from jax.sharding import PartitionSpec as P

HEAD_SIZE = 128
GCAP = 160
WIN = 53


def broadcast(x, axis, root):
    mine = lax.axis_index(axis) == root
    return lax.psum(jnp.where(mine, x, jnp.zeros_like(x)), axis)


def group_layout(prompt, count, suffix):
    offsets = jnp.arange(GCAP, dtype=jnp.int32)
    chosen_adapter_index = jnp.arange(suffix.shape[0], dtype=jnp.int32)
    live_lens = jnp.where(chosen_adapter_index < count, suffix, 0)
    end_at = prompt + jnp.cumsum(live_lens)
    group_start_rows = end_at - live_lens
    request = jnp.sum((offsets[:, None] >= end_at[None, :]).astype(jnp.int32), axis=1)
    in_prompt = offsets < prompt
    live_rows = in_prompt | (request < count)
    group_begin_row = jnp.sum(
        jnp.where(chosen_adapter_index[None, :] == request[:, None], group_start_rows[None, :], 0),
        axis=1,
    )
    position = jnp.where(in_prompt, offsets, prompt + offsets - group_begin_row)
    request_of = jnp.where(in_prompt, -1, request)
    return (live_rows, request_of, position)


def key_mask(live_rows, request_of, position):
    shared = (request_of[None, :] == -1) | (request_of[None, :] == request_of[:, None])
    causal = position[None, :] <= position[:, None]
    within = (position[:, None] - position[None, :] < WIN) | (position[None, :] == 0)
    allowed = live_rows[:, None] & live_rows[None, :] & shared & causal & within
    first_key = jnp.arange(GCAP)[None, :] == 0
    return jnp.where(live_rows[:, None], allowed, first_key)


def attention(queries, key_rows, value_rows, allowed):
    scores = jnp.einsum("qhe,khe->hqk", queries, key_rows, preferred_element_type=jnp.float32)
    scores = jnp.where(allowed[None], scores, -1e30)
    highest = jnp.max(scores, axis=2, keepdims=True)
    weights = jnp.where(allowed[None], jnp.exp(scores - highest), 0.0)
    probs = (weights / jnp.sum(weights, axis=2, keepdims=True)).astype(jnp.bfloat16)
    mixed_rows = jnp.einsum("hqk,khe->qhe", probs, value_rows, preferred_element_type=jnp.float32)
    return mixed_rows.astype(jnp.bfloat16).reshape(queries.shape[0], -1)


def rolled_blocks(x, blocks, shift):
    rows = x.shape[0]
    width = x.shape[1] // blocks
    reversed_blocks = x.reshape(rows, blocks, width)[:, ::-1, :]
    doubled = jnp.concatenate([reversed_blocks, reversed_blocks], axis=1)
    picked = lax.dynamic_slice_in_dim(doubled, blocks - 1 - shift, blocks, axis=1)
    return picked.reshape(rows, blocks * width)


def local(
    hidden,
    ln_gain,
    ln_shift,
    qkv_weight,
    qkv_bias,
    out_weight,
    out_bias,
    down_qkv,
    up_qkv,
    down_out,
    up_out,
    prompt_lens,
    suffix_lens,
    group_sizes,
    group_adapter_choice,
    chosen,
):
    row_index = lax.axis_index("row")
    col_index = lax.axis_index("col")
    row_count = lax.axis_size("row")
    col_count = lax.axis_size("col")
    adapters = chosen[group_adapter_choice]
    own_adapter = adapters[row_index]
    tokens_here, features_here = hidden.shape
    chunk = features_here // 2

    blocks_a = []
    blocks_b = []
    for shift in range(row_count):
        target_adapter = adapters[(row_index + shift) % row_count]
        payload = (
            jnp.concatenate([qkv_weight, down_qkv[target_adapter]], axis=1),
            out_weight,
        )
        if shift:
            payload = lax.ppermute(
                payload, "row", [(i, (i + shift) % row_count) for i in range(row_count)]
            )
        blocks_a.append(payload[0])
        blocks_b.append(payload[1])
    weight_a = jnp.concatenate(blocks_a, axis=0)
    weight_b = jnp.concatenate(blocks_b, axis=0)

    payload = jnp.concatenate([hidden, ln_gain[None], ln_shift[None]], axis=0)
    parity = col_index % 2
    halves = []
    for turn in range(2):
        pairs = [
            (rp * col_count + cp, (cp // 2) * col_count + 2 * rp + (turn ^ (cp % 2)))
            for rp in range(row_count)
            for cp in range(col_count)
        ]
        sent = lax.dynamic_slice_in_dim(payload, (turn ^ parity) * chunk, chunk, axis=1)
        halves.append(lax.ppermute(sent, ("row", "col"), pairs))
    first = jnp.where(parity == 0, halves[0], halves[1])
    second = jnp.where(parity == 0, halves[1], halves[0])
    mine = jnp.stack([first, second])
    gathered = lax.all_gather(mine, "col", axis=0, tiled=False)
    features = jnp.transpose(gathered[:, :, :tokens_here, :], (1, 2, 0, 3)).reshape(
        2 * tokens_here, col_count * chunk
    )
    gain_full = gathered[:, 0, tokens_here, :].reshape(-1)
    shift_full = gathered[:, 0, tokens_here + 1, :].reshape(-1)

    widened = features.astype(jnp.float32)
    average = jnp.mean(widened, axis=1, keepdims=True)
    centred = widened - average
    spread = jnp.mean(centred * centred, axis=1, keepdims=True)
    normed = (
        centred * lax.rsqrt(spread + 1e-05) * gain_full.astype(jnp.float32)
        + shift_full.astype(jnp.float32)
    ).astype(jnp.bfloat16)

    low_rank = down_qkv.shape[2]
    head_width = qkv_weight.shape[1]
    projected_all = jnp.dot(
        rolled_blocks(normed, row_count, row_index), weight_a, preferred_element_type=jnp.float32
    )
    reduced = projected_all[:, head_width:]
    projected = (
        projected_all[:, :head_width]
        + qkv_bias.astype(jnp.float32)
        + jnp.dot(
            reduced.astype(jnp.bfloat16), up_qkv[own_adapter], preferred_element_type=jnp.float32
        )
    )
    heads_here = projected.shape[1] // (3 * HEAD_SIZE)
    shaped = projected.reshape(GCAP, heads_here, 3, HEAD_SIZE)
    queries = (shaped[:, :, 0] * HEAD_SIZE ** (-0.5)).astype(jnp.bfloat16)
    key_rows = shaped[:, :, 1].astype(jnp.bfloat16)
    value_rows = shaped[:, :, 2].astype(jnp.bfloat16)
    live_rows, request_of, position = group_layout(
        prompt_lens[row_index], group_sizes[row_index], suffix_lens[row_index]
    )
    mixed_rows = attention(queries, key_rows, value_rows, key_mask(live_rows, request_of, position))
    down_here = down_out[own_adapter]
    both = lax.all_gather(
        jnp.concatenate([mixed_rows, down_here], axis=0), "col", axis=0, tiled=False
    )
    all_heads = jnp.transpose(both[:, :GCAP], (1, 0, 2)).reshape(GCAP, -1)
    down_full = jnp.transpose(both[:, GCAP:], (1, 0, 2)).reshape(low_rank, -1)
    reduced_out = lax.dot_general(
        all_heads, down_full, (((1,), (1,)), ((), ())), preferred_element_type=jnp.float32
    ).astype(jnp.bfloat16)
    combined = jnp.dot(
        rolled_blocks(all_heads, row_count, row_index), weight_b, preferred_element_type=jnp.float32
    )
    result = (
        combined
        + out_bias.astype(jnp.float32)
        + jnp.dot(reduced_out, up_out[own_adapter], preferred_element_type=jnp.float32)
    )
    return (result * live_rows[:, None].astype(jnp.float32)).astype(jnp.bfloat16)


def solution(mesh):
    in_specs = (
        P("col", "row"),
        P("row"),
        P("row"),
        P("row", "col"),
        P("col"),
        P("row", "col"),
        P("col"),
        P(None, "row", None),
        P(None, None, "col"),
        P(None, None, "col"),
        P(None, None, "col"),
        P(),
        P(),
        P(),
        P(),
        P(),
    )
    out_specs = P("row", "col")
    return jax.shard_map(local, mesh=mesh, in_specs=in_specs, out_specs=out_specs, check_vma=False)
```

```python
import jax
import jax.numpy as jnp
from jax import lax
from jax.sharding import PartitionSpec as P

HEAD_SIZE = 128
GCAP = 160
WIN = 53


def broadcast(x, axis, root):
    mine = lax.axis_index(axis) == root
    return lax.psum(jnp.where(mine, x, jnp.zeros_like(x)), axis)


def group_layout(prompt, count, suffix):
    offsets = jnp.arange(GCAP, dtype=jnp.int32)
    chosen_adapter_index = jnp.arange(suffix.shape[0], dtype=jnp.int32)
    live_lens = jnp.where(chosen_adapter_index < count, suffix, 0)
    end_at = prompt + jnp.cumsum(live_lens)
    group_start_rows = end_at - live_lens
    request = jnp.sum((offsets[:, None] >= end_at[None, :]).astype(jnp.int32), axis=1)
    in_prompt = offsets < prompt
    live_rows = in_prompt | (request < count)
    group_begin_row = jnp.sum(
        jnp.where(chosen_adapter_index[None, :] == request[:, None], group_start_rows[None, :], 0),
        axis=1,
    )
    position = jnp.where(in_prompt, offsets, prompt + offsets - group_begin_row)
    request_of = jnp.where(in_prompt, -1, request)
    return (live_rows, request_of, position)


def key_mask(live_rows, request_of, position):
    shared = (request_of[None, :] == -1) | (request_of[None, :] == request_of[:, None])
    causal = position[None, :] <= position[:, None]
    within = (position[:, None] - position[None, :] < WIN) | (position[None, :] == 0)
    allowed = live_rows[:, None] & live_rows[None, :] & shared & causal & within
    first_key = jnp.arange(GCAP)[None, :] == 0
    return jnp.where(live_rows[:, None], allowed, first_key)


def attention(queries, key_rows, value_rows, allowed):
    scores = jnp.einsum("qhe,khe->hqk", queries, key_rows, preferred_element_type=jnp.float32)
    scores = jnp.where(allowed[None], scores, -1e30)
    highest = jnp.max(scores, axis=2, keepdims=True)
    weights = jnp.where(allowed[None], jnp.exp(scores - highest), 0.0)
    probs = (weights / jnp.sum(weights, axis=2, keepdims=True)).astype(jnp.bfloat16)
    mixed_rows = jnp.einsum("hqk,khe->qhe", probs, value_rows, preferred_element_type=jnp.float32)
    return mixed_rows.astype(jnp.bfloat16).reshape(queries.shape[0], -1)


def local(
    hidden,
    ln_gain,
    ln_shift,
    qkv_weight,
    qkv_bias,
    out_weight,
    out_bias,
    down_qkv,
    up_qkv,
    down_out,
    up_out,
    prompt_lens,
    suffix_lens,
    group_sizes,
    group_adapter_choice,
    chosen,
):
    row_index = lax.axis_index("row")
    col_index = lax.axis_index("col")
    row_count = lax.axis_size("row")
    col_count = lax.axis_size("col")
    adapters = chosen[group_adapter_choice]
    own_adapter = adapters[row_index]
    tokens_here, features_here = hidden.shape
    chunk = features_here // 2
    low_rank = down_qkv.shape[2]
    head_width = qkv_weight.shape[1]
    out_rows, out_cols = out_weight.shape

    packed = jnp.concatenate(
        [qkv_weight, out_weight.reshape(features_here, -1)], axis=1
    )
    packed_full = lax.all_gather(packed, "row", axis=0, tiled=True)
    qkv_full = packed_full[:, :head_width]
    out_full = packed_full[:, head_width:].reshape(row_count * out_rows, out_cols)
    down_parts = lax.all_to_all(down_qkv[adapters], "row", 0, 0, tiled=True)
    down_full = down_parts.reshape(-1, low_rank)

    payload = jnp.concatenate([hidden, ln_gain[None], ln_shift[None]], axis=0)
    parity = col_index % 2
    halves = []
    for turn in range(2):
        pairs = [
            (rp * col_count + cp, (cp // 2) * col_count + 2 * rp + (turn ^ (cp % 2)))
            for rp in range(row_count)
            for cp in range(col_count)
        ]
        sent = lax.dynamic_slice_in_dim(payload, (turn ^ parity) * chunk, chunk, axis=1)
        halves.append(lax.ppermute(sent, ("row", "col"), pairs))
    first = jnp.where(parity == 0, halves[0], halves[1])
    second = jnp.where(parity == 0, halves[1], halves[0])
    mine = jnp.concatenate([first[:tokens_here], second], axis=0)
    gathered = lax.all_gather(mine, "col", axis=1, tiled=True)
    features = gathered[: 2 * tokens_here]
    gain_full = gathered[2 * tokens_here]
    shift_full = gathered[2 * tokens_here + 1]

    widened = features.astype(jnp.float32)
    average = jnp.mean(widened, axis=1, keepdims=True)
    centred = widened - average
    spread = jnp.mean(centred * centred, axis=1, keepdims=True)
    normed = (
        centred * lax.rsqrt(spread + 1e-05) * gain_full.astype(jnp.float32)
        + shift_full.astype(jnp.float32)
    ).astype(jnp.bfloat16)

    projected = jnp.dot(normed, qkv_full, preferred_element_type=jnp.float32)
    reduced = jnp.dot(normed, down_full, preferred_element_type=jnp.float32)
    projected = (
        projected
        + qkv_bias.astype(jnp.float32)
        + jnp.dot(
            reduced.astype(jnp.bfloat16), up_qkv[own_adapter], preferred_element_type=jnp.float32
        )
    )
    heads_here = projected.shape[1] // (3 * HEAD_SIZE)
    shaped = projected.reshape(GCAP, heads_here, 3, HEAD_SIZE)
    queries = (shaped[:, :, 0] * HEAD_SIZE ** (-0.5)).astype(jnp.bfloat16)
    key_rows = shaped[:, :, 1].astype(jnp.bfloat16)
    value_rows = shaped[:, :, 2].astype(jnp.bfloat16)
    live_rows, request_of, position = group_layout(
        prompt_lens[row_index], group_sizes[row_index], suffix_lens[row_index]
    )
    mixed_rows = attention(queries, key_rows, value_rows, key_mask(live_rows, request_of, position))
    down_here = down_out[own_adapter]
    both = lax.all_gather(
        jnp.concatenate([mixed_rows, down_here], axis=0), "col", axis=1, tiled=True
    )
    all_heads = both[:GCAP]
    down_out_full = both[GCAP:]
    reduced_out = lax.dot_general(
        all_heads, down_out_full, (((1,), (1,)), ((), ())), preferred_element_type=jnp.float32
    ).astype(jnp.bfloat16)
    combined = jnp.dot(all_heads, out_full, preferred_element_type=jnp.float32)
    result = (
        combined
        + out_bias.astype(jnp.float32)
        + jnp.dot(reduced_out, up_out[own_adapter], preferred_element_type=jnp.float32)
    )
    return (result * live_rows[:, None].astype(jnp.float32)).astype(jnp.bfloat16)


def solution(mesh):
    in_specs = (
        P("col", "row"),
        P("row"),
        P("row"),
        P("row", "col"),
        P("col"),
        P("row", "col"),
        P("col"),
        P(None, "row", None),
        P(None, None, "col"),
        P(None, None, "col"),
        P(None, None, "col"),
        P(),
        P(),
        P(),
        P(),
        P(),
    )
    out_specs = P("row", "col")
    return jax.shard_map(local, mesh=mesh, in_specs=in_specs, out_specs=out_specs, check_vma=False)
```

```python
import jax
import jax.numpy as jnp
from jax import lax
from jax.sharding import PartitionSpec as P

HEAD_SIZE = 128
GCAP = 160
WIN = 53


def group_layout(prompt, count, suffix):
    offsets = jnp.arange(GCAP, dtype=jnp.int32)
    chosen_adapter_index = jnp.arange(suffix.shape[0], dtype=jnp.int32)
    live_lens = jnp.where(chosen_adapter_index < count, suffix, 0)
    end_at = prompt + jnp.cumsum(live_lens)
    group_start_rows = end_at - live_lens
    request = jnp.sum((offsets[:, None] >= end_at[None, :]).astype(jnp.int32), axis=1)
    in_prompt = offsets < prompt
    live_rows = in_prompt | (request < count)
    group_begin_row = jnp.sum(
        jnp.where(chosen_adapter_index[None, :] == request[:, None], group_start_rows[None, :], 0),
        axis=1,
    )
    position = jnp.where(in_prompt, offsets, prompt + offsets - group_begin_row)
    request_of = jnp.where(in_prompt, -1, request)
    return (live_rows, request_of, position)


def key_mask(live_rows, request_of, position):
    shared = (request_of[None, :] == -1) | (request_of[None, :] == request_of[:, None])
    causal = position[None, :] <= position[:, None]
    within = (position[:, None] - position[None, :] < WIN) | (position[None, :] == 0)
    allowed = live_rows[:, None] & live_rows[None, :] & shared & causal & within
    first_key = jnp.arange(GCAP)[None, :] == 0
    return jnp.where(live_rows[:, None], allowed, first_key)


def attention(queries, key_rows, value_rows, allowed):
    scores = jnp.einsum("qhe,khe->hqk", queries, key_rows, preferred_element_type=jnp.float32)
    scores = jnp.where(allowed[None], scores, -1e30)
    highest = jnp.max(scores, axis=2, keepdims=True)
    weights = jnp.where(allowed[None], jnp.exp(scores - highest), 0.0)
    probs = (weights / jnp.sum(weights, axis=2, keepdims=True)).astype(jnp.bfloat16)
    mixed_rows = jnp.einsum("hqk,khe->qhe", probs, value_rows, preferred_element_type=jnp.float32)
    return mixed_rows.astype(jnp.bfloat16).reshape(queries.shape[0], -1)


def layer(
    hidden,
    ln_gain,
    ln_shift,
    qkv_weight,
    qkv_bias,
    out_weight,
    out_bias,
    down_qkv,
    up_qkv,
    down_out,
    up_out,
    prompt_lens,
    suffix_lens,
    group_sizes,
    group_adapter_choice,
    chosen,
):
    row_index = lax.axis_index("row")
    col_index = lax.axis_index("col")
    row_count = lax.axis_size("row")
    col_count = lax.axis_size("col")
    adapters = chosen[group_adapter_choice]
    own_adapter = adapters[row_index]
    tokens_here, features_here = hidden.shape
    chunk = features_here // 2
    low_rank = down_qkv.shape[2]
    head_width = qkv_weight.shape[1]
    out_rows, out_cols = out_weight.shape

    packed = jnp.concatenate(
        [qkv_weight, out_weight.reshape(features_here, -1)], axis=1
    )
    packed_full = lax.all_gather(packed, "row", axis=0, tiled=True)
    qkv_full = packed_full[:, :head_width]
    out_full = packed_full[:, head_width:].reshape(row_count * out_rows, out_cols)
    down_parts = lax.all_to_all(down_qkv[adapters], "row", 0, 0, tiled=True)
    down_full = down_parts.reshape(-1, low_rank)

    payload = jnp.concatenate([hidden, ln_gain[None], ln_shift[None]], axis=0)
    parity = col_index % 2
    halves = []
    for turn in range(2):
        pairs = [
            (rp * col_count + cp, (cp // 2) * col_count + 2 * rp + (turn ^ (cp % 2)))
            for rp in range(row_count)
            for cp in range(col_count)
        ]
        sent = lax.dynamic_slice_in_dim(payload, (turn ^ parity) * chunk, chunk, axis=1)
        halves.append(lax.ppermute(sent, ("row", "col"), pairs))
    first = jnp.where(parity == 0, halves[0], halves[1])
    second = jnp.where(parity == 0, halves[1], halves[0])
    mine = jnp.concatenate([first[:tokens_here], second], axis=0)
    gathered = lax.all_gather(mine, "col", axis=1, tiled=True)
    features = gathered[: 2 * tokens_here]
    gain_full = gathered[2 * tokens_here]
    shift_full = gathered[2 * tokens_here + 1]

    widened = features.astype(jnp.float32)
    average = jnp.mean(widened, axis=1, keepdims=True)
    centred = widened - average
    spread = jnp.mean(centred * centred, axis=1, keepdims=True)
    normed = (
        centred * lax.rsqrt(spread + 1e-05) * gain_full.astype(jnp.float32)
        + shift_full.astype(jnp.float32)
    ).astype(jnp.bfloat16)

    projected = jnp.dot(normed, qkv_full, preferred_element_type=jnp.float32)
    reduced = jnp.dot(normed, down_full, preferred_element_type=jnp.float32)
    projected = (
        projected
        + qkv_bias.astype(jnp.float32)
        + jnp.dot(
            reduced.astype(jnp.bfloat16), up_qkv[own_adapter], preferred_element_type=jnp.float32
        )
    )
    heads_here = projected.shape[1] // (3 * HEAD_SIZE)
    shaped = projected.reshape(GCAP, heads_here, 3, HEAD_SIZE)
    queries = (shaped[:, :, 0] * HEAD_SIZE ** (-0.5)).astype(jnp.bfloat16)
    key_rows = shaped[:, :, 1].astype(jnp.bfloat16)
    value_rows = shaped[:, :, 2].astype(jnp.bfloat16)
    live_rows, request_of, position = group_layout(
        prompt_lens[row_index], group_sizes[row_index], suffix_lens[row_index]
    )
    mixed_rows = attention(queries, key_rows, value_rows, key_mask(live_rows, request_of, position))
    down_here = down_out[own_adapter]
    both = lax.all_gather(
        jnp.concatenate([mixed_rows, down_here], axis=0), "col", axis=1, tiled=True
    )
    all_heads = both[:GCAP]
    down_out_full = both[GCAP:]
    reduced_out = lax.dot_general(
        all_heads, down_out_full, (((1,), (1,)), ((), ())), preferred_element_type=jnp.float32
    ).astype(jnp.bfloat16)
    combined = jnp.dot(all_heads, out_full, preferred_element_type=jnp.float32)
    result = (
        combined
        + out_bias.astype(jnp.float32)
        + jnp.dot(reduced_out, up_out[own_adapter], preferred_element_type=jnp.float32)
    )
    return (result * live_rows[:, None].astype(jnp.float32)).astype(jnp.bfloat16)


def solution(mesh):
    in_specs = (
        P("col", "row"),
        P("row"),
        P("row"),
        P("row", "col"),
        P("col"),
        P("row", "col"),
        P("col"),
        P(None, "row", None),
        P(None, None, "col"),
        P(None, None, "col"),
        P(None, None, "col"),
        P(),
        P(),
        P(),
        P(),
        P(),
    )
    out_specs = P("row", "col")
    return jax.shard_map(layer, mesh=mesh, in_specs=in_specs, out_specs=out_specs, check_vma=False)
```

```python
import jax
import jax.numpy as jnp
from jax import lax
from jax.sharding import PartitionSpec as P

HEAD_SIZE = 128
GCAP = 160
WIN = 53


def group_layout(prompt, count, suffix):
    offsets = jnp.arange(GCAP, dtype=jnp.int32)
    chosen_adapter_index = jnp.arange(suffix.shape[0], dtype=jnp.int32)
    live_lens = jnp.where(chosen_adapter_index < count, suffix, 0)
    end_at = prompt + jnp.cumsum(live_lens)
    group_start_rows = end_at - live_lens
    request = jnp.sum((offsets[:, None] >= end_at[None, :]).astype(jnp.int32), axis=1)
    in_prompt = offsets < prompt
    live_rows = in_prompt | (request < count)
    group_begin_row = jnp.sum(
        jnp.where(chosen_adapter_index[None, :] == request[:, None], group_start_rows[None, :], 0),
        axis=1,
    )
    position = jnp.where(in_prompt, offsets, prompt + offsets - group_begin_row)
    request_of = jnp.where(in_prompt, -1, request)
    return (live_rows, request_of, position)


def key_mask(live_rows, request_of, position):
    shared = (request_of[None, :] == -1) | (request_of[None, :] == request_of[:, None])
    causal = position[None, :] <= position[:, None]
    within = (position[:, None] - position[None, :] < WIN) | (position[None, :] == 0)
    allowed = live_rows[:, None] & live_rows[None, :] & shared & causal & within
    first_key = jnp.arange(GCAP)[None, :] == 0
    return jnp.where(live_rows[:, None], allowed, first_key)


def attention(queries, key_rows, value_rows, allowed):
    scores = jnp.einsum("qhe,khe->hqk", queries, key_rows, preferred_element_type=jnp.float32)
    scores = jnp.where(allowed[None], scores, -1e30)
    highest = jnp.max(scores, axis=2, keepdims=True)
    weights = jnp.where(allowed[None], jnp.exp(scores - highest), 0.0)
    probs = (weights / jnp.sum(weights, axis=2, keepdims=True)).astype(jnp.bfloat16)
    mixed_rows = jnp.einsum("hqk,khe->qhe", probs, value_rows, preferred_element_type=jnp.float32)
    return mixed_rows.astype(jnp.bfloat16).reshape(queries.shape[0], -1)


def layer(
    hidden,
    ln_gain,
    ln_shift,
    qkv_weight,
    qkv_bias,
    out_weight,
    out_bias,
    down_qkv,
    up_qkv,
    down_out,
    up_out,
    prompt_lens,
    suffix_lens,
    group_sizes,
    group_adapter_choice,
    chosen,
):
    row_index = lax.axis_index("row")
    col_index = lax.axis_index("col")
    row_count = lax.axis_size("row")
    col_count = lax.axis_size("col")
    adapters = chosen[group_adapter_choice]
    own_adapter = adapters[row_index]
    tokens_here, features_here = hidden.shape
    chunk = features_here // 2
    low_rank = down_qkv.shape[2]
    head_width = qkv_weight.shape[1]
    out_rows, out_cols = out_weight.shape

    packed = jnp.concatenate(
        [qkv_weight, out_weight.reshape(features_here, -1)], axis=1
    )
    packed_full = lax.all_gather(packed, "row", axis=0, tiled=True)
    qkv_full = packed_full[:, :head_width]
    out_full = packed_full[:, head_width:].reshape(row_count * out_rows, out_cols)
    down_parts = lax.all_to_all(down_qkv[adapters], "row", 0, 0, tiled=True)
    down_full = down_parts.reshape(-1, low_rank)

    payload = jnp.concatenate([hidden, ln_gain[None], ln_shift[None]], axis=0)
    parity = col_index % 2
    halves = []
    for turn in range(2):
        pairs = [
            (rp * col_count + cp, (cp // 2) * col_count + 2 * rp + (turn ^ (cp % 2)))
            for rp in range(row_count)
            for cp in range(col_count)
        ]
        sent = lax.dynamic_slice_in_dim(payload, (turn ^ parity) * chunk, chunk, axis=1)
        halves.append(lax.ppermute(sent, ("row", "col"), pairs))
    first = jnp.where(parity == 0, halves[0], halves[1])
    second = jnp.where(parity == 0, halves[1], halves[0])
    mine = jnp.concatenate([first[:tokens_here], second], axis=0)
    parity_groups = [list(range(p, col_count, 2)) for p in range(2)]
    own = lax.all_gather(
        mine, "col", axis=1, tiled=True, axis_index_groups=parity_groups
    )
    other = lax.ppermute(own, "col", [(i, i ^ 1) for i in range(col_count)])
    even = jnp.where(parity == 0, own, other)
    odd = jnp.where(parity == 0, other, own)
    row_count_here = mine.shape[0]
    gathered = jnp.stack(
        [even.reshape(row_count_here, -1, chunk), odd.reshape(row_count_here, -1, chunk)],
        axis=2,
    ).reshape(row_count_here, -1)
    features = gathered[: 2 * tokens_here]
    gain_full = gathered[2 * tokens_here]
    shift_full = gathered[2 * tokens_here + 1]

    widened = features.astype(jnp.float32)
    average = jnp.mean(widened, axis=1, keepdims=True)
    centred = widened - average
    spread = jnp.mean(centred * centred, axis=1, keepdims=True)
    normed = (
        centred * lax.rsqrt(spread + 1e-05) * gain_full.astype(jnp.float32)
        + shift_full.astype(jnp.float32)
    ).astype(jnp.bfloat16)

    projected = jnp.dot(normed, qkv_full, preferred_element_type=jnp.float32)
    reduced = jnp.dot(normed, down_full, preferred_element_type=jnp.float32)
    projected = (
        projected
        + qkv_bias.astype(jnp.float32)
        + jnp.dot(
            reduced.astype(jnp.bfloat16), up_qkv[own_adapter], preferred_element_type=jnp.float32
        )
    )
    heads_here = projected.shape[1] // (3 * HEAD_SIZE)
    shaped = projected.reshape(GCAP, heads_here, 3, HEAD_SIZE)
    queries = (shaped[:, :, 0] * HEAD_SIZE ** (-0.5)).astype(jnp.bfloat16)
    key_rows = shaped[:, :, 1].astype(jnp.bfloat16)
    value_rows = shaped[:, :, 2].astype(jnp.bfloat16)
    live_rows, request_of, position = group_layout(
        prompt_lens[row_index], group_sizes[row_index], suffix_lens[row_index]
    )
    mixed_rows = attention(queries, key_rows, value_rows, key_mask(live_rows, request_of, position))
    down_here = down_out[own_adapter]
    both = lax.all_gather(
        jnp.concatenate([mixed_rows, down_here], axis=0), "col", axis=1, tiled=True
    )
    all_heads = both[:GCAP]
    down_out_full = both[GCAP:]
    reduced_out = lax.dot_general(
        all_heads, down_out_full, (((1,), (1,)), ((), ())), preferred_element_type=jnp.float32
    ).astype(jnp.bfloat16)
    combined = jnp.dot(all_heads, out_full, preferred_element_type=jnp.float32)
    result = (
        combined
        + out_bias.astype(jnp.float32)
        + jnp.dot(reduced_out, up_out[own_adapter], preferred_element_type=jnp.float32)
    )
    return (result * live_rows[:, None].astype(jnp.float32)).astype(jnp.bfloat16)


def solution(mesh):
    in_specs = (
        P("col", "row"),
        P("row"),
        P("row"),
        P("row", "col"),
        P("col"),
        P("row", "col"),
        P("col"),
        P(None, "row", None),
        P(None, None, "col"),
        P(None, None, "col"),
        P(None, None, "col"),
        P(),
        P(),
        P(),
        P(),
        P(),
    )
    out_specs = P("row", "col")
    return jax.shard_map(layer, mesh=mesh, in_specs=in_specs, out_specs=out_specs, check_vma=False)
```

```python
import jax
import jax.numpy as jnp
from jax import lax
from jax.sharding import PartitionSpec as P

HEAD_SIZE = 128
GCAP = 160
WIN = 53


def group_layout(prompt, count, suffix):
    offsets = jnp.arange(GCAP, dtype=jnp.int32)
    chosen_adapter_index = jnp.arange(suffix.shape[0], dtype=jnp.int32)
    live_lens = jnp.where(chosen_adapter_index < count, suffix, 0)
    end_at = prompt + jnp.cumsum(live_lens)
    group_start_rows = end_at - live_lens
    request = jnp.sum((offsets[:, None] >= end_at[None, :]).astype(jnp.int32), axis=1)
    in_prompt = offsets < prompt
    live_rows = in_prompt | (request < count)
    group_begin_row = jnp.sum(
        jnp.where(chosen_adapter_index[None, :] == request[:, None], group_start_rows[None, :], 0),
        axis=1,
    )
    position = jnp.where(in_prompt, offsets, prompt + offsets - group_begin_row)
    request_of = jnp.where(in_prompt, -1, request)
    return (live_rows, request_of, position)


def key_mask(live_rows, request_of, position):
    shared = (request_of[None, :] == -1) | (request_of[None, :] == request_of[:, None])
    causal = position[None, :] <= position[:, None]
    within = (position[:, None] - position[None, :] < WIN) | (position[None, :] == 0)
    allowed = live_rows[:, None] & live_rows[None, :] & shared & causal & within
    first_key = jnp.arange(GCAP)[None, :] == 0
    return jnp.where(live_rows[:, None], allowed, first_key)


def attention(queries, key_rows, value_rows, allowed):
    scores = jnp.einsum("qhe,khe->hqk", queries, key_rows, preferred_element_type=jnp.float32)
    scores = jnp.where(allowed[None], scores, -1e30)
    highest = jnp.max(scores, axis=2, keepdims=True)
    weights = jnp.where(allowed[None], jnp.exp(scores - highest), 0.0)
    probs = (weights / jnp.sum(weights, axis=2, keepdims=True)).astype(jnp.bfloat16)
    mixed_rows = jnp.einsum("hqk,khe->qhe", probs, value_rows, preferred_element_type=jnp.float32)
    return mixed_rows.astype(jnp.bfloat16).reshape(queries.shape[0], -1)


def layer(
    hidden,
    ln_gain,
    ln_shift,
    qkv_weight,
    qkv_bias,
    out_weight,
    out_bias,
    down_qkv,
    up_qkv,
    down_out,
    up_out,
    prompt_lens,
    suffix_lens,
    group_sizes,
    group_adapter_choice,
    chosen,
):
    row_index = lax.axis_index("row")
    col_index = lax.axis_index("col")
    row_count = lax.axis_size("row")
    col_count = lax.axis_size("col")
    adapters = chosen[group_adapter_choice]
    own_adapter = adapters[row_index]
    tokens_here, features_here = hidden.shape
    chunk = features_here // 2
    low_rank = down_qkv.shape[2]
    head_width = qkv_weight.shape[1]
    out_rows, out_cols = out_weight.shape

    qkv_full = lax.all_gather(qkv_weight, "row", axis=0, tiled=True)
    lanes = 128
    side = jnp.concatenate(
        [
            down_qkv[adapters].reshape(row_count, -1, lanes),
            jnp.broadcast_to(
                out_weight.reshape(1, -1, lanes), (row_count, out_rows * out_cols // lanes, lanes)
            ),
        ],
        axis=1,
    )
    side_parts = lax.all_to_all(side, "row", 0, 0, tiled=True)
    down_width = features_here * low_rank // lanes
    down_full = side_parts[:, :down_width].reshape(-1, low_rank)
    out_full = side_parts[:, down_width:].reshape(row_count * out_rows, out_cols)

    payload = jnp.concatenate([hidden, ln_gain[None], ln_shift[None]], axis=0)
    parity = col_index % 2
    halves = []
    for turn in range(2):
        pairs = [
            (rp * col_count + cp, (cp // 2) * col_count + 2 * rp + (turn ^ (cp % 2)))
            for rp in range(row_count)
            for cp in range(col_count)
        ]
        sent = lax.dynamic_slice_in_dim(payload, (turn ^ parity) * chunk, chunk, axis=1)
        halves.append(lax.ppermute(sent, ("row", "col"), pairs))
    first = jnp.where(parity == 0, halves[0], halves[1])
    second = jnp.where(parity == 0, halves[1], halves[0])
    mine = jnp.concatenate([first[:tokens_here], second], axis=0)
    gathered = lax.all_gather(mine, "col", axis=0, tiled=False)
    group_tokens = 2 * tokens_here
    features = gathered[:, :group_tokens, :]
    gain_full = gathered[:, group_tokens : group_tokens + 1, :]
    shift_full = gathered[:, group_tokens + 1 : group_tokens + 2, :]

    widened = features.astype(jnp.float32)
    average = jnp.mean(widened, axis=(0, 2), keepdims=True)
    centred = widened - average
    spread = jnp.mean(centred * centred, axis=(0, 2), keepdims=True)
    normed = (
        centred * lax.rsqrt(spread + 1e-05) * gain_full.astype(jnp.float32)
        + shift_full.astype(jnp.float32)
    ).astype(jnp.bfloat16)

    chunks = gathered.shape[0]
    projected = jnp.einsum(
        "ctk,ckn->tn",
        normed,
        qkv_full.reshape(chunks, chunk, head_width),
        preferred_element_type=jnp.float32,
    )
    reduced = jnp.einsum(
        "ctk,ckn->tn",
        normed,
        down_full.reshape(chunks, chunk, low_rank),
        preferred_element_type=jnp.float32,
    )
    projected = (
        projected
        + qkv_bias.astype(jnp.float32)
        + jnp.dot(
            reduced.astype(jnp.bfloat16), up_qkv[own_adapter], preferred_element_type=jnp.float32
        )
    )
    heads_here = projected.shape[1] // (3 * HEAD_SIZE)
    shaped = projected.reshape(GCAP, heads_here, 3, HEAD_SIZE)
    queries = (shaped[:, :, 0] * HEAD_SIZE ** (-0.5)).astype(jnp.bfloat16)
    key_rows = shaped[:, :, 1].astype(jnp.bfloat16)
    value_rows = shaped[:, :, 2].astype(jnp.bfloat16)
    live_rows, request_of, position = group_layout(
        prompt_lens[row_index], group_sizes[row_index], suffix_lens[row_index]
    )
    mixed_rows = attention(queries, key_rows, value_rows, key_mask(live_rows, request_of, position))
    down_here = down_out[own_adapter]
    both = lax.all_gather(
        jnp.concatenate([mixed_rows, down_here], axis=0), "col", axis=1, tiled=True
    )
    all_heads = both[:GCAP]
    down_out_full = both[GCAP:]
    reduced_out = lax.dot_general(
        all_heads, down_out_full, (((1,), (1,)), ((), ())), preferred_element_type=jnp.float32
    ).astype(jnp.bfloat16)
    combined = jnp.dot(all_heads, out_full, preferred_element_type=jnp.float32)
    result = (
        combined
        + out_bias.astype(jnp.float32)
        + jnp.dot(reduced_out, up_out[own_adapter], preferred_element_type=jnp.float32)
    )
    return (result * live_rows[:, None].astype(jnp.float32)).astype(jnp.bfloat16)


def solution(mesh):
    in_specs = (
        P("col", "row"),
        P("row"),
        P("row"),
        P("row", "col"),
        P("col"),
        P("row", "col"),
        P("col"),
        P(None, "row", None),
        P(None, None, "col"),
        P(None, None, "col"),
        P(None, None, "col"),
        P(),
        P(),
        P(),
        P(),
        P(),
    )
    out_specs = P("row", "col")
    return jax.shard_map(layer, mesh=mesh, in_specs=in_specs, out_specs=out_specs, check_vma=False)
```

```python
import jax
import jax.numpy as jnp
from jax import lax
from jax.sharding import PartitionSpec as P

HEAD_SIZE = 128
GCAP = 160
WIN = 53


def group_layout(prompt, count, suffix):
    offsets = jnp.arange(GCAP, dtype=jnp.int32)
    chosen_adapter_index = jnp.arange(suffix.shape[0], dtype=jnp.int32)
    live_lens = jnp.where(chosen_adapter_index < count, suffix, 0)
    end_at = prompt + jnp.cumsum(live_lens)
    group_start_rows = end_at - live_lens
    request = jnp.sum((offsets[:, None] >= end_at[None, :]).astype(jnp.int32), axis=1)
    in_prompt = offsets < prompt
    live_rows = in_prompt | (request < count)
    group_begin_row = jnp.sum(
        jnp.where(chosen_adapter_index[None, :] == request[:, None], group_start_rows[None, :], 0),
        axis=1,
    )
    position = jnp.where(in_prompt, offsets, prompt + offsets - group_begin_row)
    request_of = jnp.where(in_prompt, -1, request)
    return (live_rows, request_of, position)


def key_mask(live_rows, request_of, position):
    shared = (request_of[None, :] == -1) | (request_of[None, :] == request_of[:, None])
    causal = position[None, :] <= position[:, None]
    within = (position[:, None] - position[None, :] < WIN) | (position[None, :] == 0)
    allowed = live_rows[:, None] & live_rows[None, :] & shared & causal & within
    first_key = jnp.arange(GCAP)[None, :] == 0
    return jnp.where(live_rows[:, None], allowed, first_key)


def attention(queries, key_rows, value_rows, allowed):
    scores = jnp.einsum("qhe,khe->hqk", queries, key_rows, preferred_element_type=jnp.float32)
    scores = jnp.where(allowed[None], scores, -1e30)
    highest = jnp.max(scores, axis=2, keepdims=True)
    weights = jnp.where(allowed[None], jnp.exp(scores - highest), 0.0)
    probs = (weights / jnp.sum(weights, axis=2, keepdims=True)).astype(jnp.bfloat16)
    mixed_rows = jnp.einsum("hqk,khe->qhe", probs, value_rows, preferred_element_type=jnp.float32)
    return mixed_rows.astype(jnp.bfloat16).reshape(queries.shape[0], -1)


def doubling_gather(x, axis, size):
    index = lax.axis_index(axis)
    blocks = x[None]
    step = 1
    while step < size:
        other = lax.ppermute(blocks, axis, [(i, i ^ step) for i in range(size)])
        lower = (index // step) % 2 == 0
        blocks = jnp.where(
            lower,
            jnp.concatenate([blocks, other], axis=0),
            jnp.concatenate([other, blocks], axis=0),
        )
        step *= 2
    return blocks


def layer(
    hidden,
    ln_gain,
    ln_shift,
    qkv_weight,
    qkv_bias,
    out_weight,
    out_bias,
    down_qkv,
    up_qkv,
    down_out,
    up_out,
    prompt_lens,
    suffix_lens,
    group_sizes,
    group_adapter_choice,
    chosen,
):
    row_index = lax.axis_index("row")
    col_index = lax.axis_index("col")
    row_count = lax.axis_size("row")
    col_count = lax.axis_size("col")
    adapters = chosen[group_adapter_choice]
    own_adapter = adapters[row_index]
    tokens_here, features_here = hidden.shape
    chunk = features_here // 2
    low_rank = down_qkv.shape[2]
    head_width = qkv_weight.shape[1]
    out_rows, out_cols = out_weight.shape

    packed = jnp.concatenate(
        [qkv_weight, out_weight.reshape(features_here, -1)], axis=1
    )
    packed_full = lax.all_gather(packed, "row", axis=0, tiled=True)
    qkv_full = packed_full[:, :head_width]
    out_full = packed_full[:, head_width:].reshape(row_count * out_rows, out_cols)
    down_parts = lax.all_to_all(down_qkv[adapters], "row", 0, 0, tiled=True)
    down_full = down_parts.reshape(-1, low_rank)

    payload = jnp.concatenate([hidden, ln_gain[None], ln_shift[None]], axis=0)
    parity = col_index % 2
    halves = []
    for turn in range(2):
        pairs = [
            (rp * col_count + cp, (cp // 2) * col_count + 2 * rp + (turn ^ (cp % 2)))
            for rp in range(row_count)
            for cp in range(col_count)
        ]
        sent = lax.dynamic_slice_in_dim(payload, (turn ^ parity) * chunk, chunk, axis=1)
        halves.append(lax.ppermute(sent, ("row", "col"), pairs))
    first = jnp.where(parity == 0, halves[0], halves[1])
    second = jnp.where(parity == 0, halves[1], halves[0])
    mine = jnp.concatenate([first[:tokens_here], second], axis=0)
    gathered = doubling_gather(mine, "col", col_count)
    group_tokens = 2 * tokens_here
    features = gathered[:, :group_tokens, :]
    gain_full = gathered[:, group_tokens : group_tokens + 1, :]
    shift_full = gathered[:, group_tokens + 1 : group_tokens + 2, :]

    widened = features.astype(jnp.float32)
    average = jnp.mean(widened, axis=(0, 2), keepdims=True)
    centred = widened - average
    spread = jnp.mean(centred * centred, axis=(0, 2), keepdims=True)
    normed = (
        centred * lax.rsqrt(spread + 1e-05) * gain_full.astype(jnp.float32)
        + shift_full.astype(jnp.float32)
    ).astype(jnp.bfloat16)

    chunks = gathered.shape[0]
    projected = jnp.einsum(
        "ctk,ckn->tn",
        normed,
        qkv_full.reshape(chunks, chunk, head_width),
        preferred_element_type=jnp.float32,
    )
    reduced = jnp.einsum(
        "ctk,ckn->tn",
        normed,
        down_full.reshape(chunks, chunk, low_rank),
        preferred_element_type=jnp.float32,
    )
    projected = (
        projected
        + qkv_bias.astype(jnp.float32)
        + jnp.dot(
            reduced.astype(jnp.bfloat16), up_qkv[own_adapter], preferred_element_type=jnp.float32
        )
    )
    heads_here = projected.shape[1] // (3 * HEAD_SIZE)
    shaped = projected.reshape(GCAP, heads_here, 3, HEAD_SIZE)
    queries = (shaped[:, :, 0] * HEAD_SIZE ** (-0.5)).astype(jnp.bfloat16)
    key_rows = shaped[:, :, 1].astype(jnp.bfloat16)
    value_rows = shaped[:, :, 2].astype(jnp.bfloat16)
    live_rows, request_of, position = group_layout(
        prompt_lens[row_index], group_sizes[row_index], suffix_lens[row_index]
    )
    mixed_rows = attention(queries, key_rows, value_rows, key_mask(live_rows, request_of, position))
    down_here = down_out[own_adapter]
    both = doubling_gather(jnp.concatenate([mixed_rows, down_here], axis=0), "col", col_count)
    all_heads = both[:, :GCAP]
    down_out_full = both[:, GCAP:]
    reduced_out = jnp.einsum(
        "cte,cre->tr", all_heads, down_out_full, preferred_element_type=jnp.float32
    ).astype(jnp.bfloat16)
    combined = jnp.einsum(
        "cte,cen->tn",
        all_heads,
        out_full.reshape(col_count, -1, out_cols),
        preferred_element_type=jnp.float32,
    )
    result = (
        combined
        + out_bias.astype(jnp.float32)
        + jnp.dot(reduced_out, up_out[own_adapter], preferred_element_type=jnp.float32)
    )
    return (result * live_rows[:, None].astype(jnp.float32)).astype(jnp.bfloat16)


def solution(mesh):
    in_specs = (
        P("col", "row"),
        P("row"),
        P("row"),
        P("row", "col"),
        P("col"),
        P("row", "col"),
        P("col"),
        P(None, "row", None),
        P(None, None, "col"),
        P(None, None, "col"),
        P(None, None, "col"),
        P(),
        P(),
        P(),
        P(),
        P(),
    )
    out_specs = P("row", "col")
    return jax.shard_map(layer, mesh=mesh, in_specs=in_specs, out_specs=out_specs, check_vma=False)
```

```python
import jax
import jax.numpy as jnp
from jax import lax
from jax.sharding import PartitionSpec as P

HEAD_SIZE = 128
GCAP = 160
WIN = 53


def group_layout(prompt, count, suffix):
    offsets = jnp.arange(GCAP, dtype=jnp.int32)
    chosen_adapter_index = jnp.arange(suffix.shape[0], dtype=jnp.int32)
    live_lens = jnp.where(chosen_adapter_index < count, suffix, 0)
    end_at = prompt + jnp.cumsum(live_lens)
    group_start_rows = end_at - live_lens
    request = jnp.sum((offsets[:, None] >= end_at[None, :]).astype(jnp.int32), axis=1)
    in_prompt = offsets < prompt
    live_rows = in_prompt | (request < count)
    group_begin_row = jnp.sum(
        jnp.where(chosen_adapter_index[None, :] == request[:, None], group_start_rows[None, :], 0),
        axis=1,
    )
    position = jnp.where(in_prompt, offsets, prompt + offsets - group_begin_row)
    request_of = jnp.where(in_prompt, -1, request)
    return (live_rows, request_of, position)


def key_mask(live_rows, request_of, position):
    shared = (request_of[None, :] == -1) | (request_of[None, :] == request_of[:, None])
    causal = position[None, :] <= position[:, None]
    within = (position[:, None] - position[None, :] < WIN) | (position[None, :] == 0)
    allowed = live_rows[:, None] & live_rows[None, :] & shared & causal & within
    first_key = jnp.arange(GCAP)[None, :] == 0
    return jnp.where(live_rows[:, None], allowed, first_key)


def attention(queries, key_rows, value_rows, allowed):
    scores = jnp.einsum("qhe,khe->hqk", queries, key_rows, preferred_element_type=jnp.float32)
    scores = jnp.where(allowed[None], scores, -1e30)
    highest = jnp.max(scores, axis=2, keepdims=True)
    weights = jnp.where(allowed[None], jnp.exp(scores - highest), 0.0)
    probs = (weights / jnp.sum(weights, axis=2, keepdims=True)).astype(jnp.bfloat16)
    mixed_rows = jnp.einsum("hqk,khe->qhe", probs, value_rows, preferred_element_type=jnp.float32)
    return mixed_rows.astype(jnp.bfloat16).reshape(queries.shape[0], -1)


def layer(
    hidden,
    ln_gain,
    ln_shift,
    qkv_weight,
    qkv_bias,
    out_weight,
    out_bias,
    down_qkv,
    up_qkv,
    down_out,
    up_out,
    prompt_lens,
    suffix_lens,
    group_sizes,
    group_adapter_choice,
    chosen,
):
    row_index = lax.axis_index("row")
    col_index = lax.axis_index("col")
    row_count = lax.axis_size("row")
    col_count = lax.axis_size("col")
    adapters = chosen[group_adapter_choice]
    own_adapter = adapters[row_index]
    tokens_here, features_here = hidden.shape
    chunk = features_here // 2
    low_rank = down_qkv.shape[2]
    head_width = qkv_weight.shape[1]
    out_rows, out_cols = out_weight.shape

    packed = jnp.concatenate(
        [qkv_weight, out_weight.reshape(features_here, -1)], axis=1
    )
    packed_full = lax.all_gather(packed, "row", axis=0, tiled=True)
    packed_full, down_rows = lax.optimization_barrier((packed_full, down_qkv[adapters]))
    down_parts = lax.all_to_all(down_rows, "row", 0, 0, tiled=True)
    down_full = down_parts.reshape(-1, low_rank)
    qkv_full = packed_full[:, :head_width]
    out_full = packed_full[:, head_width:].reshape(row_count * out_rows, out_cols)

    payload = jnp.concatenate([hidden, ln_gain[None], ln_shift[None]], axis=0)
    parity = col_index % 2
    halves = []
    for turn in range(2):
        pairs = [
            (rp * col_count + cp, (cp // 2) * col_count + 2 * rp + (turn ^ (cp % 2)))
            for rp in range(row_count)
            for cp in range(col_count)
        ]
        sent = lax.dynamic_slice_in_dim(payload, (turn ^ parity) * chunk, chunk, axis=1)
        halves.append(lax.ppermute(sent, ("row", "col"), pairs))
    first = jnp.where(parity == 0, halves[0], halves[1])
    second = jnp.where(parity == 0, halves[1], halves[0])
    mine = jnp.concatenate([first[:tokens_here], second], axis=0)
    gathered = lax.all_gather(mine, "col", axis=0, tiled=False)
    group_tokens = 2 * tokens_here
    features = gathered[:, :group_tokens, :]
    gain_full = gathered[:, group_tokens : group_tokens + 1, :]
    shift_full = gathered[:, group_tokens + 1 : group_tokens + 2, :]

    widened = features.astype(jnp.float32)
    average = jnp.mean(widened, axis=(0, 2), keepdims=True)
    centred = widened - average
    spread = jnp.mean(centred * centred, axis=(0, 2), keepdims=True)
    normed = (
        centred * lax.rsqrt(spread + 1e-05) * gain_full.astype(jnp.float32)
        + shift_full.astype(jnp.float32)
    ).astype(jnp.bfloat16)

    chunks = gathered.shape[0]
    projected = jnp.einsum(
        "ctk,ckn->tn",
        normed,
        qkv_full.reshape(chunks, chunk, head_width),
        preferred_element_type=jnp.float32,
    )
    reduced = jnp.einsum(
        "ctk,ckn->tn",
        normed,
        down_full.reshape(chunks, chunk, low_rank),
        preferred_element_type=jnp.float32,
    )
    projected = (
        projected
        + qkv_bias.astype(jnp.float32)
        + jnp.dot(
            reduced.astype(jnp.bfloat16), up_qkv[own_adapter], preferred_element_type=jnp.float32
        )
    )
    heads_here = projected.shape[1] // (3 * HEAD_SIZE)
    shaped = projected.reshape(GCAP, heads_here, 3, HEAD_SIZE)
    queries = (shaped[:, :, 0] * HEAD_SIZE ** (-0.5)).astype(jnp.bfloat16)
    key_rows = shaped[:, :, 1].astype(jnp.bfloat16)
    value_rows = shaped[:, :, 2].astype(jnp.bfloat16)
    live_rows, request_of, position = group_layout(
        prompt_lens[row_index], group_sizes[row_index], suffix_lens[row_index]
    )
    mixed_rows = attention(queries, key_rows, value_rows, key_mask(live_rows, request_of, position))
    down_here = down_out[own_adapter]
    both = lax.all_gather(
        jnp.concatenate([mixed_rows, down_here], axis=0), "col", axis=1, tiled=True
    )
    all_heads = both[:GCAP]
    down_out_full = both[GCAP:]
    reduced_out = lax.dot_general(
        all_heads, down_out_full, (((1,), (1,)), ((), ())), preferred_element_type=jnp.float32
    ).astype(jnp.bfloat16)
    combined = jnp.dot(all_heads, out_full, preferred_element_type=jnp.float32)
    result = (
        combined
        + out_bias.astype(jnp.float32)
        + jnp.dot(reduced_out, up_out[own_adapter], preferred_element_type=jnp.float32)
    )
    return (result * live_rows[:, None].astype(jnp.float32)).astype(jnp.bfloat16)


def solution(mesh):
    in_specs = (
        P("col", "row"),
        P("row"),
        P("row"),
        P("row", "col"),
        P("col"),
        P("row", "col"),
        P("col"),
        P(None, "row", None),
        P(None, None, "col"),
        P(None, None, "col"),
        P(None, None, "col"),
        P(),
        P(),
        P(),
        P(),
        P(),
    )
    out_specs = P("row", "col")
    return jax.shard_map(layer, mesh=mesh, in_specs=in_specs, out_specs=out_specs, check_vma=False)
```

```python
import jax
import jax.numpy as jnp
from jax import lax
from jax.sharding import PartitionSpec as P

HEAD_SIZE = 128
GCAP = 160
WIN = 53


def group_layout(prompt, count, suffix):
    offsets = jnp.arange(GCAP, dtype=jnp.int32)
    chosen_adapter_index = jnp.arange(suffix.shape[0], dtype=jnp.int32)
    live_lens = jnp.where(chosen_adapter_index < count, suffix, 0)
    end_at = prompt + jnp.cumsum(live_lens)
    group_start_rows = end_at - live_lens
    request = jnp.sum((offsets[:, None] >= end_at[None, :]).astype(jnp.int32), axis=1)
    in_prompt = offsets < prompt
    live_rows = in_prompt | (request < count)
    group_begin_row = jnp.sum(
        jnp.where(chosen_adapter_index[None, :] == request[:, None], group_start_rows[None, :], 0),
        axis=1,
    )
    position = jnp.where(in_prompt, offsets, prompt + offsets - group_begin_row)
    request_of = jnp.where(in_prompt, -1, request)
    return (live_rows, request_of, position)


def key_mask(live_rows, request_of, position):
    shared = (request_of[None, :] == -1) | (request_of[None, :] == request_of[:, None])
    causal = position[None, :] <= position[:, None]
    within = (position[:, None] - position[None, :] < WIN) | (position[None, :] == 0)
    allowed = live_rows[:, None] & live_rows[None, :] & shared & causal & within
    first_key = jnp.arange(GCAP)[None, :] == 0
    return jnp.where(live_rows[:, None], allowed, first_key)


def attention(queries, key_rows, value_rows, allowed):
    scores = jnp.einsum("qhe,khe->hqk", queries, key_rows, preferred_element_type=jnp.float32)
    scores = jnp.where(allowed[None], scores, -1e30)
    highest = jnp.max(scores, axis=2, keepdims=True)
    weights = jnp.where(allowed[None], jnp.exp(scores - highest), 0.0)
    probs = (weights / jnp.sum(weights, axis=2, keepdims=True)).astype(jnp.bfloat16)
    mixed_rows = jnp.einsum("hqk,khe->qhe", probs, value_rows, preferred_element_type=jnp.float32)
    return mixed_rows.astype(jnp.bfloat16).reshape(queries.shape[0], -1)


def layer(
    hidden,
    ln_gain,
    ln_shift,
    qkv_weight,
    qkv_bias,
    out_weight,
    out_bias,
    down_qkv,
    up_qkv,
    down_out,
    up_out,
    prompt_lens,
    suffix_lens,
    group_sizes,
    group_adapter_choice,
    chosen,
):
    row_index = lax.axis_index("row")
    col_index = lax.axis_index("col")
    row_count = lax.axis_size("row")
    col_count = lax.axis_size("col")
    adapters = chosen[group_adapter_choice]
    own_adapter = adapters[row_index]
    tokens_here, features_here = hidden.shape
    chunk = features_here // 2
    low_rank = down_qkv.shape[2]
    head_width = qkv_weight.shape[1]
    out_rows, out_cols = out_weight.shape

    packed = jnp.concatenate(
        [qkv_weight, out_weight.reshape(features_here, -1)], axis=1
    )
    packed_full = lax.all_gather(packed, "row", axis=0, tiled=True)
    qkv_full = packed_full[:, :head_width]
    out_full = packed_full[:, head_width:].reshape(row_count * out_rows, out_cols)
    down_parts = lax.all_to_all(down_qkv[adapters], "row", 0, 0, tiled=True)
    down_full = down_parts.reshape(-1, low_rank)

    payload = jnp.concatenate([hidden, ln_gain[None], ln_shift[None]], axis=0)
    parity = col_index % 2
    halves = []
    for turn in range(2):
        pairs = [
            (rp * col_count + cp, (cp // 2) * col_count + 2 * rp + (turn ^ (cp % 2)))
            for rp in range(row_count)
            for cp in range(col_count)
        ]
        sent = lax.dynamic_slice_in_dim(payload, (turn ^ parity) * chunk, chunk, axis=1)
        halves.append(lax.ppermute(sent, ("row", "col"), pairs))
    first = jnp.where(parity == 0, halves[0], halves[1])
    second = jnp.where(parity == 0, halves[1], halves[0])
    mine = jnp.concatenate([first[:tokens_here], second], axis=0)
    gathered = lax.all_gather(mine, "col", axis=0, tiled=False)
    group_tokens = 2 * tokens_here
    features = gathered[:, :group_tokens, :]
    gain_full = gathered[:, group_tokens : group_tokens + 1, :]
    shift_full = gathered[:, group_tokens + 1 : group_tokens + 2, :]

    widened = features.astype(jnp.float32)
    average = jnp.mean(widened, axis=(0, 2), keepdims=True)
    centred = widened - average
    spread = jnp.mean(centred * centred, axis=(0, 2), keepdims=True)
    normed = (
        centred * lax.rsqrt(spread + 1e-05) * gain_full.astype(jnp.float32)
        + shift_full.astype(jnp.float32)
    ).astype(jnp.bfloat16)

    chunks = gathered.shape[0]
    joined = jnp.concatenate([qkv_full, down_full], axis=1)
    projected_all = jnp.einsum(
        "ctk,ckn->tn",
        normed,
        joined.reshape(chunks, chunk, head_width + low_rank),
        preferred_element_type=jnp.float32,
    )
    projected = projected_all[:, :head_width]
    reduced = projected_all[:, head_width:]
    projected = (
        projected
        + qkv_bias.astype(jnp.float32)
        + jnp.dot(
            reduced.astype(jnp.bfloat16), up_qkv[own_adapter], preferred_element_type=jnp.float32
        )
    )
    heads_here = projected.shape[1] // (3 * HEAD_SIZE)
    shaped = projected.reshape(GCAP, heads_here, 3, HEAD_SIZE)
    queries = (shaped[:, :, 0] * HEAD_SIZE ** (-0.5)).astype(jnp.bfloat16)
    key_rows = shaped[:, :, 1].astype(jnp.bfloat16)
    value_rows = shaped[:, :, 2].astype(jnp.bfloat16)
    live_rows, request_of, position = group_layout(
        prompt_lens[row_index], group_sizes[row_index], suffix_lens[row_index]
    )
    mixed_rows = attention(queries, key_rows, value_rows, key_mask(live_rows, request_of, position))
    down_here = down_out[own_adapter]
    both = lax.all_gather(
        jnp.concatenate([mixed_rows, down_here], axis=0), "col", axis=1, tiled=True
    )
    all_heads = both[:GCAP]
    down_out_full = both[GCAP:]
    reduced_out = lax.dot_general(
        all_heads, down_out_full, (((1,), (1,)), ((), ())), preferred_element_type=jnp.float32
    ).astype(jnp.bfloat16)
    combined = jnp.dot(all_heads, out_full, preferred_element_type=jnp.float32)
    result = (
        combined
        + out_bias.astype(jnp.float32)
        + jnp.dot(reduced_out, up_out[own_adapter], preferred_element_type=jnp.float32)
    )
    return (result * live_rows[:, None].astype(jnp.float32)).astype(jnp.bfloat16)


def solution(mesh):
    in_specs = (
        P("col", "row"),
        P("row"),
        P("row"),
        P("row", "col"),
        P("col"),
        P("row", "col"),
        P("col"),
        P(None, "row", None),
        P(None, None, "col"),
        P(None, None, "col"),
        P(None, None, "col"),
        P(),
        P(),
        P(),
        P(),
        P(),
    )
    out_specs = P("row", "col")
    return jax.shard_map(layer, mesh=mesh, in_specs=in_specs, out_specs=out_specs, check_vma=False)
```
